512 devices in a mesh: node: 32 (over x, y), tile: 16 (over z, core).
Axes of the slice: x: 4, y: 8, z: 8, core: 2. Of those that a mesh axis runs over, the one named last changes fastest.
Arguments:
- states: bfloat16 [196608, 128], P(('node', 'tile')), may hold values from -6 to 6
- adjacency: bfloat16 [65536, 128, 128], P(('node', 'tile')), may hold values from -0.5 to 0.5
- tile_node: int32 [512, 128], P(('node', 'tile')), may hold values from 0 to 31
- tile_block: int32 [512, 128], P(('node', 'tile')), may hold values from 0 to 1, as said below
- tile_rel: int32 [512, 128], P(('node', 'tile')), may hold values from 0 to 534
- tile_dst: int32 [512, 128], P(('node', 'tile')), may hold values from 0 to 47
- send_blocks: int32 [512, 32, 2], P(('node', 'tile')), may hold values from 0 to 2
- send_count: int32 [512, 32], P(('node', 'tile')), may hold values from 1 to 2, as said below
- active: int32 [2, 1536], P(None, ('node', 'tile')), may hold values 0 or 1
- relations: bfloat16 [535, 128], replicated, may hold values from -6 to 6
- mix_weight: bfloat16 [2, 64, 64], replicated, may hold values from -0.75 to 0.75
- norm_gain: float32 [2, 64], replicated, may hold values from 0.5 to 1.5
Outputs:
- new_states: bfloat16 [196608, 128], P(('node', 'tile'))
The draws below stay inside these ranges and needn't reach their ends.
Inputs may be any that keep to these rules, and one draw needn't show every extreme that they name: On each device, the first send_count entries of each list are distinct; every device has one list with all 2 slots used. For tile t of device n * 16 + j, tile_block[d, t] is less than send_count[a * 16 + j, n], where a = tile_node[d, t].
All inputs are finite; a program needn't handle non-finite values. No bound on the sum of `active` on one device may be relied on, other than what follows from the above.
Results may differ from the reference program's by a relative error of at most 0.02.
Values may be sent and summed in bfloat16 or wider, within the bound.
No kernel may reach another device: no remote copies, remote signals or barrier semaphores. Data moves between devices by JAX's collectives and lax.ppermute only.
A program may use at most 64 MiB of HBM per device.

```python
import jax
import jax.numpy as jnp
from jax import lax

BS = 128
DIM = 64
NREL = 535
Q = 2
BLK_DEV = 3
TILES_DEV = 128
ITERS = 2
CAP = 2
BLK_NODE = 48
NBLK = 1536
ENT = 196608
N_NODE = 32
N_TILE = 16
DEVICES = 512


def joint_lists(key):
    key_count = jax.random.fold_in(key, 11)
    key_order = jax.random.fold_in(key, 12)
    key_node = jax.random.fold_in(key, 13)
    key_slot = jax.random.fold_in(key, 14)
    device_count = N_NODE * N_TILE
    counts = jax.random.randint(key_count, (device_count, N_NODE), 1, CAP + 1)
    device_iota = jnp.arange(device_count, dtype=jnp.int32)
    node_iota = jnp.arange(N_NODE, dtype=jnp.int32)
    counts = jnp.where(node_iota[None, :] == (device_iota % N_NODE)[:, None], CAP, counts).astype(jnp.int32)
    scores = jax.random.randint(key_order, (device_count, N_NODE, BLK_DEV), 0, 1 << 20) * BLK_DEV + jnp.arange(BLK_DEV, dtype=jnp.int32)
    chosen = jnp.argsort(scores, axis=-1, stable=True)[..., :CAP].astype(jnp.int32)
    home_node = device_iota // N_TILE
    column = device_iota % N_TILE
    source_node = jax.random.randint(key_node, (device_count, TILES_DEV), 0, N_NODE).astype(jnp.int32)
    sender = source_node * N_TILE + column[:, None]
    limits = counts[sender, home_node[:, None]]
    slot_index = jax.random.randint(key_slot, (device_count, TILES_DEV), 0, limits).astype(jnp.int32)
    return (counts, chosen, source_node, slot_index)


def draw_send_count(key, part):
    return joint_lists(key)[0]


def draw_send_blocks(key, part):
    return joint_lists(key)[1]


def draw_tile_node(key, part):
    return joint_lists(key)[2]


def draw_tile_block(key, part):
    return joint_lists(key)[3]


def with_ends(result, key, smallest, high):
    index_at = [jax.random.randint(jax.random.fold_in(key, axis), (), 0, length) for axis, length in enumerate(result.shape)]
    main_axis = result.shape.index(max(result.shape))
    neighbour = index_at[:main_axis] + [(index_at[main_axis] + 1) % result.shape[main_axis]] + index_at[main_axis + 1:]
    return result.at[tuple(index_at)].set(smallest).at[tuple(neighbour)].set(high)


def block_scale(own_key, dims, cuts, least, high):
    gain, own = 1.0, jax.random.fold_in(own_key, 6)
    for dim, parts in cuts:
        draws = jnp.exp(jax.random.uniform(jax.random.fold_in(own, dim), (parts,), jnp.float32, least / len(cuts), high / len(cuts)))
        gain = gain * jnp.repeat(draws, dims[dim] // parts).reshape([-1 if axis == dim else 1 for axis in range(len(dims))])
    return gain


def gaussian(key, shape, scale, reach, cuts=(), kind=jnp.bfloat16):
    values = jax.random.normal(key, shape, jnp.float32) * scale
    if len(cuts) > 0:
        values = block_scale(key, shape, cuts, -0.22, 0.18) * values
    return jnp.clip(values, min=-reach, max=reach).astype(kind)


def setup_inputs(seed: int = 0) -> dict:
    splits = jax.random.split(jax.random.key(seed), 13)
    states = gaussian(splits[0], (ENT, Q * DIM), 1.0, 6.0, ((0, 512),))
    adjacency = gaussian(splits[1], (DEVICES * TILES_DEV, BS, BS), BS ** -0.5, 0.5, ((0, 512),))
    tile_node = draw_tile_node(jax.random.fold_in(splits[12], 71), 0)
    tile_block = draw_tile_block(jax.random.fold_in(splits[12], 71), 0)
    tile_rel = with_ends(jax.random.randint(splits[4], (DEVICES, TILES_DEV), 0, NREL), jax.random.fold_in(splits[4], 1), 0, NREL - 1).astype(jnp.int32)
    tile_dst = with_ends(jax.random.randint(splits[5], (DEVICES, TILES_DEV), 0, BLK_NODE), jax.random.fold_in(splits[5], 1), 0, BLK_NODE - 1).astype(jnp.int32)
    send_blocks = draw_send_blocks(jax.random.fold_in(splits[12], 71), 0)
    send_count = draw_send_count(jax.random.fold_in(splits[12], 71), 0)
    active = with_ends((jax.random.randint(splits[8], (ITERS, NBLK), 0, 4) < 3).astype(jnp.int32), jax.random.fold_in(splits[8], 1), 0, 1)
    relations = gaussian(splits[9], (NREL, Q * DIM), 1.0, 6.0)
    mix_weight = gaussian(splits[10], (ITERS, DIM, DIM), DIM ** -0.5, 0.75)
    norm_gain = jnp.clip(1.0 + 0.1 * jax.random.normal(splits[11], (ITERS, DIM), jnp.float32), 0.5, 1.5)
    return dict(states=states, adjacency=adjacency, tile_node=tile_node, tile_block=tile_block, tile_rel=tile_rel, tile_dst=tile_dst, send_blocks=send_blocks, send_count=send_count, active=active, relations=relations, mix_weight=mix_weight, norm_gain=norm_gain)


def reference(states, adjacency, tile_node, tile_block, tile_rel, tile_dst, send_blocks, send_count, active, relations, mix_weight, norm_gain):
    width = Q * DIM
    total_blocks = BLK_DEV * N_NODE * N_TILE
    group_blocks = BLK_DEV * N_TILE
    adj_all = adjacency.reshape(N_NODE, N_TILE, TILES_DEV, BS, BS)
    node_all = tile_node.reshape(N_NODE, N_TILE, TILES_DEV)
    slot_all = tile_block.reshape(N_NODE, N_TILE, TILES_DEV)
    tile_iota = jnp.arange(N_TILE, dtype=jnp.int32)
    group_iota = jnp.arange(N_NODE, dtype=jnp.int32)[:, None, None]
    sender_all = (node_all * N_TILE + tile_iota[None, :, None]).astype(jnp.int32)
    local_all = send_blocks[sender_all, group_iota, slot_all].astype(jnp.int32)
    valid_all = (slot_all < send_count[sender_all, group_iota]).astype(jnp.float32)
    source_all = (sender_all * BLK_DEV + local_all).astype(jnp.int32)
    rel_all = relations.astype(jnp.float32)[tile_rel.reshape(N_NODE, N_TILE, TILES_DEV)] * valid_all[..., None]
    dst_all = tile_dst.reshape(N_NODE, N_TILE, TILES_DEV)
    for layer in range(ITERS):
        blocks = states.reshape(total_blocks, BS, width) * active[layer][:, None, None].astype(jnp.bfloat16)

        def one_group(group_args):

            def one_device(total, inner):
                adj_dev, source_dev, rel_dev, dst_dev = inner
                modulated = (blocks[source_dev].astype(jnp.float32) * rel_dev[:, None, :]).astype(jnp.bfloat16)
                products = jnp.einsum('tij,tjf->tif', adj_dev.astype(jnp.float32), modulated.astype(jnp.float32), precision=lax.Precision.HIGHEST)
                partial_sum = jax.ops.segment_sum(products, dst_dev, num_segments=group_blocks)
                partial_sum = lax.optimization_barrier(partial_sum.astype(jnp.bfloat16)).astype(jnp.float32)
                return (total + partial_sum, None)
            start = jnp.zeros((group_blocks, BS, width), jnp.float32)
            total, _ = lax.scan(one_device, start, group_args)
            return total
        summed = lax.map(one_group, (adj_all, source_all, rel_all, dst_all))
        summed = summed.reshape(total_blocks * BS, Q, DIM).astype(jnp.bfloat16)
        mixed = jnp.einsum('rqd,de->rqe', summed.astype(jnp.float32), mix_weight[layer].astype(jnp.float32), precision=lax.Precision.HIGHEST)
        center = lax.optimization_barrier(jnp.mean(mixed, axis=-1, keepdims=True))
        spread = lax.optimization_barrier(jnp.mean(jnp.square(mixed - center), axis=-1, keepdims=True))
        normed = (mixed - center) * lax.rsqrt(spread + 1e-05) * norm_gain[layer]
        states = (states.astype(jnp.float32) + jax.nn.relu(normed).reshape(-1, width)).astype(jnp.bfloat16)
    return states
```

```python
import jax
import jax.numpy as jnp
import numpy as np
from jax import lax
from jax.sharding import Mesh
from jax.sharding import PartitionSpec as P

NODE_AXES = ("x", "y")
TILE_AXES = ("z", "core")
ALL_AXES = NODE_AXES + TILE_AXES


def body(
    states,
    adjacency,
    tile_node,
    tile_block,
    tile_rel,
    tile_dst,
    send_blocks,
    send_count,
    active,
    relations,
    mix_weight,
    norm_gain,
):
    size_block = adjacency.shape[1]
    width = states.shape[1]
    own_blocks = states.shape[0] // size_block
    n_z = lax.axis_size("z")
    n_core = lax.axis_size("core")
    group_blocks = own_blocks * n_z * n_core
    tiles_here = adjacency.shape[0]
    depth = mix_weight.shape[1]
    query_count = width // depth
    me_node = lax.axis_index("x") * lax.axis_size("y") + lax.axis_index("y")

    lists_all = lax.all_gather(send_blocks[0], NODE_AXES, axis=0, tiled=False)
    counts_all = lax.all_gather(send_count[0], NODE_AXES, axis=0, tiled=False)
    lists_mine = lax.dynamic_index_in_dim(lists_all, me_node, axis=1, keepdims=False)
    counts_mine = lax.dynamic_index_in_dim(counts_all, me_node, axis=1, keepdims=False)
    sender = tile_node[0]
    slot = tile_block[0]
    local_block = jnp.clip(lists_mine[sender, slot], 0, own_blocks - 1)
    valid = (slot < counts_mine[sender]).astype(jnp.float32)
    source_index = sender * own_blocks + local_block

    rel_onehot = (
        tile_rel[0][:, None] == jnp.arange(relations.shape[0], dtype=jnp.int32)[None, :]
    ).astype(jnp.bfloat16)
    rel_rows = jnp.dot(rel_onehot, relations, preferred_element_type=jnp.float32)
    rel_rows = rel_rows * valid[:, None]
    dst_onehot = (
        jnp.arange(group_blocks, dtype=jnp.int32)[:, None] == tile_dst[0][None, :]
    ).astype(jnp.bfloat16)
    for layer in range(mix_weight.shape[0]):
        blocks = states.reshape(own_blocks, size_block, width) * active[layer][
            :, None, None
        ].astype(jnp.bfloat16)
        gathered = lax.all_gather(blocks, NODE_AXES, axis=0, tiled=True)
        source_rows = jnp.take(gathered, source_index, axis=0)
        modulated = (source_rows * rel_rows[:, None, :]).astype(jnp.bfloat16)
        products = jnp.einsum(
            "tij,tjf->tif", adjacency, modulated, preferred_element_type=jnp.float32
        )
        flat_products = products.reshape(tiles_here, -1)
        high_part = flat_products.astype(jnp.bfloat16)
        low_part = (flat_products - high_part.astype(jnp.float32)).astype(jnp.bfloat16)
        partial_sum = jnp.dot(dst_onehot, high_part, preferred_element_type=jnp.float32) + jnp.dot(
            dst_onehot, low_part, preferred_element_type=jnp.float32
        )
        partial_sum = partial_sum.astype(jnp.bfloat16).reshape(
            n_z, n_core, own_blocks * size_block, width
        )
        by_core = jnp.swapaxes(partial_sum, 0, 1).reshape(-1, width)
        half = lax.psum_scatter(by_core, "core", scatter_dimension=0, tiled=True)
        summed = lax.psum_scatter(half, "z", scatter_dimension=0, tiled=True)
        mixer = jnp.kron(jnp.eye(query_count, dtype=jnp.bfloat16), mix_weight[layer])
        mixed = jnp.dot(summed, mixer, preferred_element_type=jnp.float32).reshape(
            -1, query_count, depth
        )
        center = jnp.mean(mixed, axis=-1, keepdims=True)
        spread = jnp.mean(jnp.square(mixed - center), axis=-1, keepdims=True)
        normed = (mixed - center) * lax.rsqrt(spread + 1e-05) * norm_gain[layer]
        states = (states.astype(jnp.float32) + jax.nn.relu(normed).reshape(-1, width)).astype(
            jnp.bfloat16
        )
    return states


def solution(mesh):
    n_node, n_tile = mesh.devices.shape
    n_x = 4 if n_node % 4 == 0 else 1
    n_y = n_node // n_x
    fine = Mesh(np.asarray(mesh.devices).reshape(n_x, n_y, n_tile // 2, 2), ALL_AXES)
    rows = P(ALL_AXES, None)
    placed = (
        rows,
        P(ALL_AXES, None, None),
        rows,
        rows,
        rows,
        rows,
        P(ALL_AXES, None, None),
        rows,
        P(None, ALL_AXES),
        P(),
        P(),
        P(),
    )
    return jax.shard_map(body, mesh=fine, in_specs=placed, out_specs=rows, check_vma=False)
```

```python
import jax
import jax.numpy as jnp
from jax import lax
from jax.sharding import PartitionSpec as P


def body(
    states,
    adjacency,
    tile_node,
    tile_block,
    tile_rel,
    tile_dst,
    send_blocks,
    send_count,
    active,
    relations,
    mix_weight,
    norm_gain,
):
    size_block = adjacency.shape[1]
    width = states.shape[1]
    own_blocks = states.shape[0] // size_block
    group_blocks = own_blocks * lax.axis_size("tile")
    tiles_here = adjacency.shape[0]
    capacity = send_blocks.shape[2]
    depth = mix_weight.shape[1]
    query_count = width // depth
    rel_onehot = (
        tile_rel[0][:, None] == jnp.arange(relations.shape[0], dtype=jnp.int32)[None, :]
    ).astype(jnp.bfloat16)
    rel_rows = jnp.dot(rel_onehot, relations, preferred_element_type=jnp.float32)
    dst_onehot = (
        jnp.arange(group_blocks, dtype=jnp.int32)[:, None] == tile_dst[0][None, :]
    ).astype(jnp.bfloat16)
    for layer in range(mix_weight.shape[0]):
        blocks = states.reshape(own_blocks, size_block, width) * active[layer][
            :, None, None
        ].astype(jnp.bfloat16)
        usable = jnp.arange(capacity, dtype=jnp.int32)[None, :] < send_count[0][:, None]
        picked = jnp.take(blocks, send_blocks[0], axis=0)
        picked = jnp.where(usable[:, :, None, None], picked, jnp.zeros_like(picked))
        arrived = lax.all_to_all(picked, "node", split_axis=0, concat_axis=0, tiled=True)
        slot_index = tile_node[0] * capacity + tile_block[0]
        source = arrived.reshape(-1, size_block, width)
        source_rows = jnp.take(source, slot_index, axis=0)
        modulated = (source_rows * rel_rows[:, None, :]).astype(jnp.bfloat16)
        products = jnp.einsum(
            "tij,tjf->tif", adjacency, modulated, preferred_element_type=jnp.float32
        )
        flat_products = products.reshape(tiles_here, -1)
        high_part = flat_products.astype(jnp.bfloat16)
        low_part = (flat_products - high_part.astype(jnp.float32)).astype(jnp.bfloat16)
        partial_sum = jnp.dot(dst_onehot, high_part, preferred_element_type=jnp.float32) + jnp.dot(
            dst_onehot, low_part, preferred_element_type=jnp.float32
        )
        partial_sum = partial_sum.astype(jnp.bfloat16).reshape(
            lax.axis_size("tile"), own_blocks * size_block, width
        )
        received = lax.all_to_all(partial_sum, "tile", split_axis=0, concat_axis=0, tiled=True)
        summed = jnp.sum(received.astype(jnp.float32), axis=0).astype(jnp.bfloat16)
        mixer = jnp.kron(jnp.eye(query_count, dtype=jnp.bfloat16), mix_weight[layer])
        mixed = jnp.dot(summed, mixer, preferred_element_type=jnp.float32).reshape(
            -1, query_count, depth
        )
        center = jnp.mean(mixed, axis=-1, keepdims=True)
        spread = jnp.mean(jnp.square(mixed - center), axis=-1, keepdims=True)
        normed = (mixed - center) * lax.rsqrt(spread + 1e-05) * norm_gain[layer]
        states = (states.astype(jnp.float32) + jax.nn.relu(normed).reshape(-1, width)).astype(
            jnp.bfloat16
        )
    return states


def solution(mesh):
    placed = (
        P(("node", "tile"), None),
        P(("node", "tile"), None, None),
        P(("node", "tile"), None),
        P(("node", "tile"), None),
        P(("node", "tile"), None),
        P(("node", "tile"), None),
        P(("node", "tile"), None, None),
        P(("node", "tile"), None),
        P(None, ("node", "tile")),
        P(),
        P(),
        P(),
    )
    return jax.shard_map(
        body, mesh=mesh, in_specs=placed, out_specs=P(("node", "tile"), None), check_vma=False
    )
```

```python
import jax
import jax.numpy as jnp
from jax import lax
from jax.sharding import PartitionSpec as P


def body(
    states,
    adjacency,
    tile_node,
    tile_block,
    tile_rel,
    tile_dst,
    send_blocks,
    send_count,
    active,
    relations,
    mix_weight,
    norm_gain,
):
    size_block = adjacency.shape[1]
    width = states.shape[1]
    own_blocks = states.shape[0] // size_block
    n_tile = lax.axis_size("tile")
    group_blocks = own_blocks * n_tile
    tiles_here = adjacency.shape[0]
    capacity = send_blocks.shape[2]
    depth = mix_weight.shape[1]
    query_count = width // depth
    lanes = 128
    rel_onehot = (
        tile_rel[0][:, None] == jnp.arange(relations.shape[0], dtype=jnp.int32)[None, :]
    ).astype(jnp.bfloat16)
    rel_rows = jnp.dot(rel_onehot, relations, preferred_element_type=jnp.float32)
    dst_onehot = (
        jnp.arange(group_blocks, dtype=jnp.int32)[:, None] == tile_dst[0][None, :]
    ).astype(jnp.bfloat16)
    usable = jnp.arange(capacity, dtype=jnp.int32)[None, :] < send_count[0][:, None]
    slot_index = tile_node[0] * capacity + tile_block[0]

    def one_layer(h, layer, rel_part):
        blocks = h.reshape(own_blocks, size_block, depth) * active[layer][
            :, None, None
        ].astype(jnp.bfloat16)
        picked = jnp.take(blocks, send_blocks[0], axis=0)
        picked = jnp.where(usable[:, :, None, None], picked, jnp.zeros_like(picked))
        lead = picked.shape[:2]
        picked = picked.reshape(lead + (size_block * depth // lanes, lanes))
        arrived = lax.all_to_all(picked, "node", split_axis=0, concat_axis=0, tiled=True)
        source = arrived.reshape(-1, size_block, depth)
        source_rows = jnp.take(source, slot_index, axis=0)
        modulated = (source_rows * rel_part[:, None, :]).astype(jnp.bfloat16)
        products = jnp.einsum(
            "tij,tjf->tif", adjacency, modulated, preferred_element_type=jnp.float32
        )
        flat_products = products.reshape(tiles_here, -1)
        high_part = flat_products.astype(jnp.bfloat16)
        low_part = (flat_products - high_part.astype(jnp.float32)).astype(jnp.bfloat16)
        partial_sum = jnp.dot(dst_onehot, high_part, preferred_element_type=jnp.float32) + jnp.dot(
            dst_onehot, low_part, preferred_element_type=jnp.float32
        )
        partial_sum = partial_sum.astype(jnp.bfloat16).reshape(
            n_tile, own_blocks * size_block * depth // lanes, lanes
        )
        received = lax.all_to_all(partial_sum, "tile", split_axis=0, concat_axis=0, tiled=True)
        summed = jnp.sum(received.astype(jnp.float32), axis=0).astype(jnp.bfloat16)
        summed = summed.reshape(own_blocks * size_block, depth)
        mixed = jnp.dot(summed, mix_weight[layer], preferred_element_type=jnp.float32)
        center = jnp.mean(mixed, axis=-1, keepdims=True)
        spread = jnp.mean(jnp.square(mixed - center), axis=-1, keepdims=True)
        normed = (mixed - center) * lax.rsqrt(spread + 1e-05) * norm_gain[layer]
        return (h.astype(jnp.float32) + jax.nn.relu(normed)).astype(jnp.bfloat16)

    halves = []
    for query in range(query_count):
        columns = slice(query * depth, (query + 1) * depth)
        h = states[:, columns]
        rel_part = rel_rows[:, columns]
        for layer in range(mix_weight.shape[0]):
            h = one_layer(h, layer, rel_part)
        halves.append(h)
    return jnp.concatenate(halves, axis=1)


def solution(mesh):
    placed = (
        P(("node", "tile"), None),
        P(("node", "tile"), None, None),
        P(("node", "tile"), None),
        P(("node", "tile"), None),
        P(("node", "tile"), None),
        P(("node", "tile"), None),
        P(("node", "tile"), None, None),
        P(("node", "tile"), None),
        P(None, ("node", "tile")),
        P(),
        P(),
        P(),
    )
    return jax.shard_map(
        body, mesh=mesh, in_specs=placed, out_specs=P(("node", "tile"), None), check_vma=False
    )
```

```python
import jax
import jax.numpy as jnp
from jax import lax
from jax.sharding import PartitionSpec as P


def body(
    states,
    adjacency,
    tile_node,
    tile_block,
    tile_rel,
    tile_dst,
    send_blocks,
    send_count,
    active,
    relations,
    mix_weight,
    norm_gain,
):
    size_block = adjacency.shape[1]
    width = states.shape[1]
    own_blocks = states.shape[0] // size_block
    group_blocks = own_blocks * lax.axis_size("tile")
    tiles_here = adjacency.shape[0]
    capacity = send_blocks.shape[2]
    depth = mix_weight.shape[1]
    query_count = width // depth
    rel_onehot = (
        tile_rel[0][:, None] == jnp.arange(relations.shape[0], dtype=jnp.int32)[None, :]
    ).astype(jnp.bfloat16)
    rel_rows = jnp.dot(rel_onehot, relations, preferred_element_type=jnp.float32)
    dst_onehot = (
        jnp.arange(group_blocks, dtype=jnp.int32)[:, None] == tile_dst[0][None, :]
    ).astype(jnp.bfloat16)
    for layer in range(mix_weight.shape[0]):
        blocks = states.reshape(own_blocks, size_block, width) * active[layer][
            :, None, None
        ].astype(jnp.bfloat16)
        usable = jnp.arange(capacity, dtype=jnp.int32)[None, :] < send_count[0][:, None]
        picked = jnp.take(blocks, send_blocks[0], axis=0)
        picked = jnp.where(usable[:, :, None, None], picked, jnp.zeros_like(picked))
        arrived = lax.all_to_all(picked, "node", split_axis=0, concat_axis=0, tiled=True)
        slot_index = tile_node[0] * capacity + tile_block[0]
        source = arrived.reshape(-1, size_block, width)
        source_rows = jnp.take(source, slot_index, axis=0)
        modulated = (source_rows * rel_rows[:, None, :]).astype(jnp.bfloat16)
        products = jnp.einsum(
            "tij,tjf->tif", adjacency, modulated, preferred_element_type=jnp.float32
        )
        high_part = products.astype(jnp.bfloat16)
        low_part = (products - high_part.astype(jnp.float32)).astype(jnp.bfloat16)
        partial_sum = jnp.einsum(
            "mt,tif->mif", dst_onehot, high_part, preferred_element_type=jnp.float32
        ) + jnp.einsum("mt,tif->mif", dst_onehot, low_part, preferred_element_type=jnp.float32)
        partial_sum = partial_sum.astype(jnp.bfloat16).reshape(
            lax.axis_size("tile"), own_blocks * size_block, width
        )
        received = lax.all_to_all(partial_sum, "tile", split_axis=0, concat_axis=0, tiled=True)
        summed = jnp.sum(received.astype(jnp.float32), axis=0).astype(jnp.bfloat16)
        mixer = jnp.kron(jnp.eye(query_count, dtype=jnp.bfloat16), mix_weight[layer])
        mixed = jnp.dot(summed, mixer, preferred_element_type=jnp.float32).reshape(
            -1, query_count, depth
        )
        center = jnp.mean(mixed, axis=-1, keepdims=True)
        spread = jnp.mean(jnp.square(mixed - center), axis=-1, keepdims=True)
        normed = (mixed - center) * lax.rsqrt(spread + 1e-05) * norm_gain[layer]
        states = (states.astype(jnp.float32) + jax.nn.relu(normed).reshape(-1, width)).astype(
            jnp.bfloat16
        )
    return states


def solution(mesh):
    placed = (
        P(("node", "tile"), None),
        P(("node", "tile"), None, None),
        P(("node", "tile"), None),
        P(("node", "tile"), None),
        P(("node", "tile"), None),
        P(("node", "tile"), None),
        P(("node", "tile"), None, None),
        P(("node", "tile"), None),
        P(None, ("node", "tile")),
        P(),
        P(),
        P(),
    )
    return jax.shard_map(
        body, mesh=mesh, in_specs=placed, out_specs=P(("node", "tile"), None), check_vma=False
    )
```

```python
import jax
import jax.numpy as jnp
from jax import lax
from jax.sharding import PartitionSpec as P


def body(
    states,
    adjacency,
    tile_node,
    tile_block,
    tile_rel,
    tile_dst,
    send_blocks,
    send_count,
    active,
    relations,
    mix_weight,
    norm_gain,
):
    size_block = adjacency.shape[1]
    width = states.shape[1]
    own_blocks = states.shape[0] // size_block
    group_blocks = own_blocks * lax.axis_size("tile")
    tiles_here = adjacency.shape[0]
    capacity = send_blocks.shape[2]
    depth = mix_weight.shape[1]
    query_count = width // depth
    rel_onehot = (
        tile_rel[0][:, None] == jnp.arange(relations.shape[0], dtype=jnp.int32)[None, :]
    ).astype(jnp.bfloat16)
    rel_rows = jnp.dot(rel_onehot, relations, preferred_element_type=jnp.float32)
    dst_onehot = (
        jnp.arange(group_blocks, dtype=jnp.int32)[:, None] == tile_dst[0][None, :]
    ).astype(jnp.bfloat16)
    for layer in range(mix_weight.shape[0]):
        blocks = states.reshape(own_blocks, size_block, width) * active[layer][
            :, None, None
        ].astype(jnp.bfloat16)
        usable = jnp.arange(capacity, dtype=jnp.int32)[None, :] < send_count[0][:, None]
        picked = jnp.take(blocks, send_blocks[0], axis=0)
        picked = jnp.where(usable[:, :, None, None], picked, jnp.zeros_like(picked))
        arrived = lax.all_to_all(picked, "node", split_axis=0, concat_axis=0, tiled=True)
        slot_index = tile_node[0] * capacity + tile_block[0]
        source = arrived.reshape(-1, size_block, width)
        source_rows = jnp.take(source, slot_index, axis=0)
        modulated = (source_rows * rel_rows[:, None, :]).astype(jnp.bfloat16)
        products = jnp.einsum(
            "tij,tjf->tfi", adjacency, modulated, preferred_element_type=jnp.float32
        )
        flat_products = products.reshape(tiles_here, -1)
        high_part = flat_products.astype(jnp.bfloat16)
        low_part = (flat_products - high_part.astype(jnp.float32)).astype(jnp.bfloat16)
        partial_sum = jnp.dot(dst_onehot, high_part, preferred_element_type=jnp.float32) + jnp.dot(
            dst_onehot, low_part, preferred_element_type=jnp.float32
        )
        partial_sum = partial_sum.astype(jnp.bfloat16).reshape(
            lax.axis_size("tile"), own_blocks, width, size_block
        )
        received = lax.all_to_all(partial_sum, "tile", split_axis=0, concat_axis=0, tiled=True)
        summed = jnp.sum(received.astype(jnp.float32), axis=0).astype(jnp.bfloat16)
        summed = jnp.swapaxes(summed, 1, 2).reshape(own_blocks * size_block, width)
        mixer = jnp.kron(jnp.eye(query_count, dtype=jnp.bfloat16), mix_weight[layer])
        mixed = jnp.dot(summed, mixer, preferred_element_type=jnp.float32).reshape(
            -1, query_count, depth
        )
        center = jnp.mean(mixed, axis=-1, keepdims=True)
        spread = jnp.mean(jnp.square(mixed - center), axis=-1, keepdims=True)
        normed = (mixed - center) * lax.rsqrt(spread + 1e-05) * norm_gain[layer]
        states = (states.astype(jnp.float32) + jax.nn.relu(normed).reshape(-1, width)).astype(
            jnp.bfloat16
        )
    return states


def solution(mesh):
    placed = (
        P(("node", "tile"), None),
        P(("node", "tile"), None, None),
        P(("node", "tile"), None),
        P(("node", "tile"), None),
        P(("node", "tile"), None),
        P(("node", "tile"), None),
        P(("node", "tile"), None, None),
        P(("node", "tile"), None),
        P(None, ("node", "tile")),
        P(),
        P(),
        P(),
    )
    return jax.shard_map(
        body, mesh=mesh, in_specs=placed, out_specs=P(("node", "tile"), None), check_vma=False
    )
```

```python
import jax
import jax.numpy as jnp
from jax import lax
from jax.sharding import PartitionSpec as P


def body(
    states,
    adjacency,
    tile_node,
    tile_block,
    tile_rel,
    tile_dst,
    send_blocks,
    send_count,
    active,
    relations,
    mix_weight,
    norm_gain,
):
    size_block = adjacency.shape[1]
    width = states.shape[1]
    own_blocks = states.shape[0] // size_block
    group_blocks = own_blocks * lax.axis_size("tile")
    tiles_here = adjacency.shape[0]
    capacity = send_blocks.shape[2]
    depth = mix_weight.shape[1]
    query_count = width // depth
    rel_onehot = (
        tile_rel[0][:, None] == jnp.arange(relations.shape[0], dtype=jnp.int32)[None, :]
    ).astype(jnp.bfloat16)
    rel_rows = jnp.dot(rel_onehot, relations, preferred_element_type=jnp.float32)
    dst_onehot = (
        jnp.arange(group_blocks, dtype=jnp.int32)[:, None] == tile_dst[0][None, :]
    ).astype(jnp.bfloat16)
    for layer in range(mix_weight.shape[0]):
        blocks = states.reshape(own_blocks, size_block, width) * active[layer][
            :, None, None
        ].astype(jnp.bfloat16)
        usable = jnp.arange(capacity, dtype=jnp.int32)[None, :] < send_count[0][:, None]
        picked = jnp.take(blocks, send_blocks[0], axis=0)
        picked = jnp.where(usable[:, :, None, None], picked, jnp.zeros_like(picked))
        arrived = lax.all_to_all(picked, "node", split_axis=0, concat_axis=0, tiled=True)
        slot_index = tile_node[0] * capacity + tile_block[0]
        source = arrived.reshape(-1, size_block, width)
        source_rows = jnp.take(source, slot_index, axis=0)
        modulated = (source_rows * rel_rows[:, None, :]).astype(jnp.bfloat16)
        products = jnp.einsum(
            "tij,tjf->tfi", adjacency, modulated, preferred_element_type=jnp.float32
        )
        flat_products = products.reshape(tiles_here, -1)
        partial_sum = jnp.dot(
            dst_onehot, flat_products.astype(jnp.bfloat16), preferred_element_type=jnp.float32
        )
        partial_sum = partial_sum.astype(jnp.bfloat16).reshape(
            lax.axis_size("tile"), own_blocks, width, size_block
        )
        received = lax.all_to_all(partial_sum, "tile", split_axis=0, concat_axis=0, tiled=True)
        summed = jnp.sum(received.astype(jnp.float32), axis=0).astype(jnp.bfloat16)
        summed = jnp.swapaxes(summed, 1, 2).reshape(own_blocks * size_block, width)
        mixer = jnp.kron(jnp.eye(query_count, dtype=jnp.bfloat16), mix_weight[layer])
        mixed = jnp.dot(summed, mixer, preferred_element_type=jnp.float32).reshape(
            -1, query_count, depth
        )
        center = jnp.mean(mixed, axis=-1, keepdims=True)
        spread = jnp.mean(jnp.square(mixed - center), axis=-1, keepdims=True)
        normed = (mixed - center) * lax.rsqrt(spread + 1e-05) * norm_gain[layer]
        states = (states.astype(jnp.float32) + jax.nn.relu(normed).reshape(-1, width)).astype(
            jnp.bfloat16
        )
    return states


def solution(mesh):
    placed = (
        P(("node", "tile"), None),
        P(("node", "tile"), None, None),
        P(("node", "tile"), None),
        P(("node", "tile"), None),
        P(("node", "tile"), None),
        P(("node", "tile"), None),
        P(("node", "tile"), None, None),
        P(("node", "tile"), None),
        P(None, ("node", "tile")),
        P(),
        P(),
        P(),
    )
    return jax.shard_map(
        body, mesh=mesh, in_specs=placed, out_specs=P(("node", "tile"), None), check_vma=False
    )
```

```python
import jax
import jax.numpy as jnp
from jax import lax
from jax.sharding import PartitionSpec as P


def body(
    states,
    adjacency,
    tile_node,
    tile_block,
    tile_rel,
    tile_dst,
    send_blocks,
    send_count,
    active,
    relations,
    mix_weight,
    norm_gain,
):
    size_block = adjacency.shape[1]
    width = states.shape[1]
    own_blocks = states.shape[0] // size_block
    group_blocks = own_blocks * lax.axis_size("tile")
    tiles_here = adjacency.shape[0]
    capacity = send_blocks.shape[2]
    depth = mix_weight.shape[1]
    query_count = width // depth
    rel_onehot = (
        tile_rel[0][:, None] == jnp.arange(relations.shape[0], dtype=jnp.int32)[None, :]
    ).astype(jnp.bfloat16)
    rel_rows = jnp.dot(rel_onehot, relations, preferred_element_type=jnp.float32)
    dst_onehot = (
        jnp.arange(group_blocks, dtype=jnp.int32)[:, None] == tile_dst[0][None, :]
    ).astype(jnp.bfloat16)
    for layer in range(mix_weight.shape[0]):
        blocks = states.reshape(own_blocks, size_block, width) * active[layer][
            :, None, None
        ].astype(jnp.bfloat16)
        usable = jnp.arange(capacity, dtype=jnp.int32)[None, :] < send_count[0][:, None]
        picked = jnp.take(blocks, send_blocks[0], axis=0)
        picked = jnp.where(usable[:, :, None, None], picked, jnp.zeros_like(picked))
        arrived = lax.all_to_all(picked, "node", split_axis=0, concat_axis=0, tiled=True)
        slot_index = tile_node[0] * capacity + tile_block[0]
        source = arrived.reshape(-1, size_block, width)
        source_rows = jnp.take(source, slot_index, axis=0)
        modulated = (source_rows * rel_rows[:, None, :]).astype(jnp.bfloat16)
        products = jnp.einsum(
            "tij,tjf->tfi", adjacency, modulated, preferred_element_type=jnp.float32
        )
        flat_products = products.reshape(tiles_here, -1)
        partial_sum = jnp.dot(
            dst_onehot, flat_products.astype(jnp.bfloat16), preferred_element_type=jnp.float32
        )
        partial_sum = partial_sum.astype(jnp.bfloat16).reshape(
            lax.axis_size("tile"), own_blocks, width, size_block
        )
        received = lax.all_to_all(
            partial_sum[:, : own_blocks - 1], "tile", split_axis=0, concat_axis=0, tiled=True
        )
        summed_head = jnp.sum(received.astype(jnp.float32), axis=0).astype(jnp.bfloat16)
        summed_tail = lax.psum_scatter(
            partial_sum[:, own_blocks - 1].reshape(-1, size_block),
            "tile",
            scatter_dimension=0,
            tiled=True,
        )
        summed = jnp.concatenate([summed_head, summed_tail[None]], axis=0)
        summed = jnp.swapaxes(summed, 1, 2).reshape(own_blocks * size_block, width)
        mixer = jnp.kron(jnp.eye(query_count, dtype=jnp.bfloat16), mix_weight[layer])
        mixed = jnp.dot(summed, mixer, preferred_element_type=jnp.float32).reshape(
            -1, query_count, depth
        )
        center = jnp.mean(mixed, axis=-1, keepdims=True)
        spread = jnp.mean(jnp.square(mixed - center), axis=-1, keepdims=True)
        normed = (mixed - center) * lax.rsqrt(spread + 1e-05) * norm_gain[layer]
        states = (states.astype(jnp.float32) + jax.nn.relu(normed).reshape(-1, width)).astype(
            jnp.bfloat16
        )
    return states


def solution(mesh):
    placed = (
        P(("node", "tile"), None),
        P(("node", "tile"), None, None),
        P(("node", "tile"), None),
        P(("node", "tile"), None),
        P(("node", "tile"), None),
        P(("node", "tile"), None),
        P(("node", "tile"), None, None),
        P(("node", "tile"), None),
        P(None, ("node", "tile")),
        P(),
        P(),
        P(),
    )
    return jax.shard_map(
        body, mesh=mesh, in_specs=placed, out_specs=P(("node", "tile"), None), check_vma=False
    )
```

```python
import jax
import jax.numpy as jnp
from jax import lax
from jax.sharding import PartitionSpec as P


def body(
    states,
    adjacency,
    tile_node,
    tile_block,
    tile_rel,
    tile_dst,
    send_blocks,
    send_count,
    active,
    relations,
    mix_weight,
    norm_gain,
):
    size_block = adjacency.shape[1]
    width = states.shape[1]
    own_blocks = states.shape[0] // size_block
    group_blocks = own_blocks * lax.axis_size("tile")
    tiles_here = adjacency.shape[0]
    capacity = send_blocks.shape[2]
    depth = mix_weight.shape[1]
    query_count = width // depth
    rel_onehot = (
        tile_rel[0][:, None] == jnp.arange(relations.shape[0], dtype=jnp.int32)[None, :]
    ).astype(jnp.bfloat16)
    rel_rows = jnp.dot(rel_onehot, relations, preferred_element_type=jnp.float32)
    dst_onehot = (
        jnp.arange(group_blocks, dtype=jnp.int32)[:, None] == tile_dst[0][None, :]
    ).astype(jnp.bfloat16)
    usable = jnp.arange(capacity, dtype=jnp.int32)[None, :] < send_count[0][:, None]
    pick_index = jnp.where(usable, jnp.clip(send_blocks[0], 0, own_blocks - 1), own_blocks)
    for layer in range(mix_weight.shape[0]):
        blocks = states.reshape(own_blocks, size_block, width) * active[layer][
            :, None, None
        ].astype(jnp.bfloat16)
        with_zero = jnp.concatenate([blocks, jnp.zeros_like(blocks[:1])], axis=0)
        picked = jnp.take(with_zero, pick_index, axis=0)
        arrived = lax.all_to_all(picked, "node", split_axis=0, concat_axis=0, tiled=True)
        slot_index = tile_node[0] * capacity + tile_block[0]
        source = arrived.reshape(-1, size_block, width)
        source_rows = jnp.take(source, slot_index, axis=0)
        modulated = (source_rows * rel_rows[:, None, :]).astype(jnp.bfloat16)
        products = jnp.einsum(
            "tij,tjf->tfi", adjacency, modulated, preferred_element_type=jnp.float32
        )
        flat_products = products.reshape(tiles_here, -1)
        partial_sum = jnp.dot(
            dst_onehot, flat_products.astype(jnp.bfloat16), preferred_element_type=jnp.float32
        )
        partial_sum = partial_sum.astype(jnp.bfloat16).reshape(
            lax.axis_size("tile"), own_blocks, width, size_block
        )
        received = lax.all_to_all(partial_sum, "tile", split_axis=0, concat_axis=0, tiled=True)
        summed = jnp.sum(received.astype(jnp.float32), axis=0).astype(jnp.bfloat16)
        summed = jnp.swapaxes(summed, 1, 2).reshape(own_blocks * size_block, width)
        mixer = jnp.kron(jnp.eye(query_count, dtype=jnp.bfloat16), mix_weight[layer])
        mixed = jnp.dot(summed, mixer, preferred_element_type=jnp.float32).reshape(
            -1, query_count, depth
        )
        center = jnp.mean(mixed, axis=-1, keepdims=True)
        spread = jnp.mean(jnp.square(mixed - center), axis=-1, keepdims=True)
        normed = (mixed - center) * lax.rsqrt(spread + 1e-05) * norm_gain[layer]
        states = (states.astype(jnp.float32) + jax.nn.relu(normed).reshape(-1, width)).astype(
            jnp.bfloat16
        )
    return states


def solution(mesh):
    placed = (
        P(("node", "tile"), None),
        P(("node", "tile"), None, None),
        P(("node", "tile"), None),
        P(("node", "tile"), None),
        P(("node", "tile"), None),
        P(("node", "tile"), None),
        P(("node", "tile"), None, None),
        P(("node", "tile"), None),
        P(None, ("node", "tile")),
        P(),
        P(),
        P(),
    )
    return jax.shard_map(
        body, mesh=mesh, in_specs=placed, out_specs=P(("node", "tile"), None), check_vma=False
    )
```
